256 devices in a mesh: row: 8 (over z_lo, x), rep: 32 (over z_hi, y, core).
Axes of the slice: x: 4, y: 4, z: 8 (z_hi: 4, z_lo: 2; z = z_hi * 2 + z_lo), core: 2. Of those that a mesh axis runs over, the one named last changes fastest.
Arguments:
- features: bfloat16 [32768, 128], P(('row', 'rep')), may hold values from -6 to 6
- block_values: bfloat16 [32768, 128, 128], P(('row', 'rep')), may hold values from -0.078125 to 0.078125
- block_rows: int32 [256, 128], P(('row', 'rep')), may hold values from 0 to 31, as said below
- block_cols: int32 [256, 128], P(('row', 'rep')), may hold values from 0 to 7, as said below
- block_count: int32 [256], replicated, may hold values from 16 to 128, as said below
- weight: bfloat16 [128, 256], replicated, may hold values from -0.5 to 0.5
- bias: float32 [256], replicated, may hold values from -3 to 3
Outputs:
- output: bfloat16 [32768, 256], P(('row', 'rep'))
The draws below stay inside these ranges and needn't reach their ends.
Inputs may be any that keep to these rules, and one draw needn't show every extreme that they name: `block_rows`: no two slots of one device name the same row block and column section. `block_cols`: with block_rows, no two slots of one device name the same pair. `block_count`: the live slots of a device are its first ones; some device has all 128 slots live.
All inputs are finite; a program needn't handle non-finite values.
Results may differ from the reference program's by a relative error of at most 0.0046.
Values may be sent and summed in bfloat16 or wider, within the bound.
No kernel may reach another device: no remote copies, remote signals or barrier semaphores. Data moves between devices by JAX's collectives and lax.ppermute only.
A program may use at most 64 MiB of HBM per device.

```python
import jax
import jax.numpy as jnp
from jax import lax

F_IN = 128
HID = 256
BLK = 128
KB = 128
NODES = 32768
N_ROW = 8
N_REP = 32


def slot_table(key):
    devices = N_ROW * N_REP
    pair_total = N_REP * N_ROW
    key_local, key_far = jax.random.split(jax.random.fold_in(key, 11))
    device = jnp.arange(devices, dtype=jnp.int32)[:, None]
    pair_index = jnp.arange(pair_total, dtype=jnp.int32)[None, :]
    row_block = pair_index // N_ROW
    section_of = pair_index % N_ROW
    own_row = device // N_REP
    own_rep = device % N_REP
    distance = jnp.abs(row_block - own_rep)
    distance = jnp.minimum(distance, N_REP - distance)
    jitter = jax.random.randint(key_local, (devices, pair_total), 0, 4)
    spread = jax.random.randint(key_far, (devices, pair_total), 0, 2 * N_REP)
    ranking = jnp.where(section_of == own_row, 2 * distance + jitter, spread)
    ranking = ranking * pair_total + pair_index
    chosen = jnp.argsort(ranking, axis=1)[:, :KB]
    return ((chosen // N_ROW).astype(jnp.int32), (chosen % N_ROW).astype(jnp.int32))


def draw_block_rows(key, part):
    return slot_table(key)[0]


def draw_block_cols(key, part):
    return slot_table(key)[1]


def draw_block_count(key, part):
    devices = N_ROW * N_REP
    key_light, key_heavy, key_load, key_full = jax.random.split(jax.random.fold_in(key, 29), 4)
    light_load = jax.random.randint(key_light, (devices,), max(KB // 8, 1), KB // 2 + 1)
    heavy_mask = jax.random.randint(key_heavy, (devices,), 0, 8) == 0
    heavy_load = jax.random.randint(key_load, (devices,), 3 * KB // 4, KB + 1)
    full_device = jax.random.randint(key_full, (), 0, devices)
    loads = jnp.where(heavy_mask, heavy_load, light_load)
    loads = jnp.where(jnp.arange(devices, dtype=jnp.int32) == full_device, KB, loads)
    return loads.astype(jnp.int32)


def levels(own_key, shape, cuts, smallest, largest):
    def one(position, parts):
        draws = jax.random.uniform(jax.random.fold_in(jax.random.fold_in(own_key, 6), position), (parts,), jnp.float32, smallest / len(cuts), largest / len(cuts))
        return jnp.repeat(jnp.exp(draws), shape[position] // parts).reshape((-1,) + (1,) * (len(shape) - position - 1))

    level = one(*cuts[0])
    for cut in cuts[1:]:
        level = level * one(*cut)
    return level


def centred(own_key, dims, scale, bound, cuts=(), held_as=jnp.bfloat16):
    factor_of = levels(own_key, dims, cuts, -0.22, 0.18) if cuts else 1.0
    result = jax.random.normal(own_key, dims, jnp.float32) * scale * factor_of
    return jnp.minimum(jnp.maximum(result, -bound), bound).astype(held_as)


def setup_inputs(seed: int = 0) -> dict:
    key_list = jax.random.split(jax.random.key(seed), 8)
    features = centred(key_list[0], (NODES, F_IN), 1.0, 6.0, ((0, 256),))
    block_values = centred(key_list[1], (KB * N_ROW * N_REP, BLK, BLK), (KB * BLK // 3) ** -0.5, 0.078125, ((0, 256),))
    block_rows = draw_block_rows(jax.random.fold_in(key_list[7], 71), 0)
    block_cols = draw_block_cols(jax.random.fold_in(key_list[7], 71), 0)
    block_count = draw_block_count(jax.random.fold_in(key_list[7], 71), 0)
    weight = centred(key_list[5], (F_IN, HID), F_IN ** -0.5, 0.5)
    bias = centred(key_list[6], (HID,), 0.5, 3.0, (), jnp.float32)
    return {"features": features, "block_values": block_values, "block_rows": block_rows, "block_cols": block_cols, "block_count": block_count, "weight": weight, "bias": bias}


def reference(features, block_values, block_rows, block_cols, block_count, weight, bias):
    devices = N_ROW * N_REP
    slot_total = block_rows.shape[1]
    node_blocks = features.reshape(devices, BLK, F_IN)
    block_sets = block_values.reshape(devices, slot_total, BLK, BLK)
    slot_index = jnp.arange(slot_total, dtype=jnp.int32)

    def one_device(totals, inputs):
        device_index, block_set, row_slots, section_slots, live_count = inputs
        row_index = (device_index // N_REP).astype(jnp.int32)
        rep_index = (device_index % N_REP).astype(jnp.int32)
        sources = (section_slots * N_REP + rep_index).astype(jnp.int32)
        gathered = node_blocks[sources].astype(jnp.float32)
        contribution = jnp.einsum("kij,kjf->kif", block_set.astype(jnp.float32), gathered)
        contribution = jnp.where((slot_index < live_count)[:, None, None], contribution, jnp.float32(0.0))
        slab_sums = jnp.zeros((N_REP, BLK, F_IN), jnp.float32).at[row_slots.astype(jnp.int32)].add(contribution)
        return totals.at[row_index].add(slab_sums), None

    initial = jnp.zeros((N_ROW, N_REP, BLK, F_IN), jnp.float32)
    device_ids = jnp.arange(devices, dtype=jnp.int32)
    totals, _ = lax.scan(one_device, initial, (device_ids, block_sets, block_rows, block_cols, block_count))
    aggregated = totals.reshape(devices * BLK, F_IN)
    aggregated_bf = aggregated.astype(jnp.bfloat16)
    projected = jnp.dot(aggregated_bf, weight, preferred_element_type=jnp.float32) + bias
    return jax.nn.relu(projected).astype(jnp.bfloat16)
```

```python
import functools

import jax
import jax.numpy as jnp
from jax import lax
from jax.experimental import pallas as pl
from jax.experimental.pallas import tpu as pltpu
from jax.sharding import PartitionSpec as P

GROUP = 16


def slot_kernel(rows_ref, cols_ref, count_ref, feats_ref, vals_ref, out_ref):
    g = pl.program_id(0)
    live = count_ref[0]

    @pl.when(g == 0)
    def _():
        out_ref[...] = jnp.zeros_like(out_ref)

    for s in range(GROUP):
        k = g * GROUP + s

        @pl.when(k < live)
        def _():
            r = rows_ref[k]
            c = cols_ref[k]
            out_ref[r] += jnp.dot(
                vals_ref[s], feats_ref[c], preferred_element_type=jnp.float32
            )


def accumulate_slots(rows, cols, count, feats, vals, rep_size):
    slot_total, blk, _ = vals.shape
    sections, _, width = feats.shape
    groups = slot_total // GROUP

    def vals_map(g, rows_ref, cols_ref, count_ref):
        last = jnp.maximum(count_ref[0] - 1, 0) // GROUP
        return (jnp.minimum(g, last), 0, 0)

    grid_spec = pltpu.PrefetchScalarGridSpec(
        num_scalar_prefetch=3,
        grid=(groups,),
        in_specs=[
            pl.BlockSpec((sections, blk, width), lambda g, *_: (0, 0, 0)),
            pl.BlockSpec((GROUP, blk, blk), vals_map),
        ],
        out_specs=pl.BlockSpec((rep_size, blk, width), lambda g, *_: (0, 0, 0)),
    )
    return pl.pallas_call(
        slot_kernel,
        grid_spec=grid_spec,
        out_shape=jax.ShapeDtypeStruct((rep_size, blk, width), jnp.float32),
        compiler_params=pltpu.CompilerParams(dimension_semantics=("arbitrary",)),
        cost_estimate=pl.CostEstimate(
            flops=2 * slot_total * blk * blk * width,
            bytes_accessed=vals.size * 2 + feats.size * 2 + rep_size * blk * width * 4,
            transcendentals=0,
        ),
    )(rows, cols, count, feats, vals)


def per_device(features, block_values, block_rows, block_cols, block_count, weight, bias):
    block_size = features.shape[0]
    feature_width = features.shape[1]
    rep_size = lax.axis_size("rep")
    section_features = lax.all_gather(features, "row", axis=0, tiled=True).reshape(
        -1, block_size, feature_width
    )
    device_index = lax.axis_index(("row", "rep"))
    live_count = lax.dynamic_slice_in_dim(block_count, device_index, 1, 0)
    partial_value = accumulate_slots(
        block_rows[0], block_cols[0], live_count, section_features, block_values, rep_size
    )
    summed = lax.psum_scatter(
        partial_value.reshape(rep_size * block_size, feature_width),
        "rep",
        scatter_dimension=0,
        tiled=True,
    )
    reduced = summed.astype(jnp.bfloat16)
    projected = jnp.dot(reduced, weight, preferred_element_type=jnp.float32) + bias
    return jax.nn.relu(projected).astype(jnp.bfloat16)


def solution(mesh):
    return jax.shard_map(
        per_device,
        mesh=mesh,
        in_specs=(
            P(("row", "rep"), None),
            P(("row", "rep"), None, None),
            P(("row", "rep"), None),
            P(("row", "rep"), None),
            P(),
            P(),
            P(),
        ),
        out_specs=P(("row", "rep"), None),
        check_vma=False,
    )
```

```python
import functools

import jax
import jax.numpy as jnp
from jax import lax
from jax.experimental import pallas as pl
from jax.experimental.pallas import tpu as pltpu
from jax.sharding import PartitionSpec as P

GROUP = 16


def slot_kernel(rows_ref, cols_ref, count_ref, feats_ref, vals_ref, out_ref):
    g = pl.program_id(0)
    live = count_ref[0]

    @pl.when(g == 0)
    def _():
        out_ref[...] = jnp.zeros_like(out_ref)

    for s in range(GROUP):
        k = g * GROUP + s

        @pl.when(k < live)
        def _():
            r = rows_ref[k]
            c = cols_ref[k]
            out_ref[r] += jnp.dot(
                vals_ref[s], feats_ref[c], preferred_element_type=jnp.float32
            )


def accumulate_slots(rows, cols, count, feats, vals, rep_size):
    slot_total, blk, _ = vals.shape
    sections, _, width = feats.shape
    groups = slot_total // GROUP

    def vals_map(g, rows_ref, cols_ref, count_ref):
        last = jnp.maximum(count_ref[0] - 1, 0) // GROUP
        return (jnp.minimum(g, last), 0, 0)

    grid_spec = pltpu.PrefetchScalarGridSpec(
        num_scalar_prefetch=3,
        grid=(groups,),
        in_specs=[
            pl.BlockSpec((sections, blk, width), lambda g, *_: (0, 0, 0)),
            pl.BlockSpec((GROUP, blk, blk), vals_map),
        ],
        out_specs=pl.BlockSpec((rep_size, blk, width), lambda g, *_: (0, 0, 0)),
    )
    return pl.pallas_call(
        slot_kernel,
        grid_spec=grid_spec,
        out_shape=jax.ShapeDtypeStruct((rep_size, blk, width), jnp.float32),
        compiler_params=pltpu.CompilerParams(dimension_semantics=("arbitrary",)),
        cost_estimate=pl.CostEstimate(
            flops=2 * slot_total * blk * blk * width,
            bytes_accessed=vals.size * 2 + feats.size * 2 + rep_size * blk * width * 4,
            transcendentals=0,
        ),
    )(rows, cols, count, feats, vals)


def reduce_over_rep(x):
    rep_size = x.shape[0]
    j = lax.axis_index("rep")
    c = j % 2
    y = (j // 2) % 4
    z = j // 8
    x = x.reshape((rep_size // 8, 4, 2) + x.shape[1:])
    keep = lax.dynamic_index_in_dim(x, c, 2, keepdims=False)
    send = lax.dynamic_index_in_dim(x, 1 - c, 2, keepdims=False)
    x = keep + lax.ppermute(send, "rep", [(i, i ^ 1) for i in range(rep_size)])
    acc = lax.dynamic_index_in_dim(x, y, 1, keepdims=False)
    for d in (1, 2, 3):
        send = lax.dynamic_index_in_dim(x, (y + d) % 4, 1, keepdims=False)
        perm = [(i, (i // 8) * 8 + (((i // 2) % 4 + d) % 4) * 2 + i % 2) for i in range(rep_size)]
        acc = acc + lax.ppermute(send, "rep", perm)
    x = acc
    z_size = x.shape[0]
    acc = lax.dynamic_index_in_dim(x, z, 0, keepdims=False)
    for d in range(1, z_size):
        send = lax.dynamic_index_in_dim(x, (z + d) % z_size, 0, keepdims=False)
        perm = [(i, (((i // 8) + d) % z_size) * 8 + i % 8) for i in range(rep_size)]
        acc = acc + lax.ppermute(send, "rep", perm)
    return acc


def per_device(features, block_values, block_rows, block_cols, block_count, weight, bias):
    block_size = features.shape[0]
    feature_width = features.shape[1]
    rep_size = lax.axis_size("rep")
    section_features = lax.all_gather(features, "row", axis=0, tiled=True).reshape(
        -1, block_size, feature_width
    )
    device_index = lax.axis_index(("row", "rep"))
    live_count = lax.dynamic_slice_in_dim(block_count, device_index, 1, 0)
    partial_value = accumulate_slots(
        block_rows[0], block_cols[0], live_count, section_features, block_values, rep_size
    )
    summed = reduce_over_rep(partial_value)
    reduced = summed.astype(jnp.bfloat16)
    projected = jnp.dot(reduced, weight, preferred_element_type=jnp.float32) + bias
    return jax.nn.relu(projected).astype(jnp.bfloat16)


def solution(mesh):
    return jax.shard_map(
        per_device,
        mesh=mesh,
        in_specs=(
            P(("row", "rep"), None),
            P(("row", "rep"), None, None),
            P(("row", "rep"), None),
            P(("row", "rep"), None),
            P(),
            P(),
            P(),
        ),
        out_specs=P(("row", "rep"), None),
        check_vma=False,
    )
```

```python
import functools

import jax
import jax.numpy as jnp
from jax import lax
from jax.experimental import pallas as pl
from jax.experimental.pallas import tpu as pltpu
from jax.sharding import PartitionSpec as P

GROUP = 16


def slot_kernel(rows_ref, cols_ref, count_ref, feats_ref, vals_ref, out_ref):
    g = pl.program_id(0)
    live = count_ref[0]

    @pl.when(g == 0)
    def _():
        out_ref[...] = jnp.zeros_like(out_ref)

    for s in range(GROUP):
        k = g * GROUP + s

        @pl.when(k < live)
        def _():
            r = rows_ref[k]
            c = cols_ref[k]
            out_ref[r] += jnp.dot(
                vals_ref[s], feats_ref[c], preferred_element_type=jnp.float32
            )


def accumulate_slots(rows, cols, count, feats, vals, rep_size):
    slot_total, blk, _ = vals.shape
    sections, _, width = feats.shape
    groups = slot_total // GROUP

    def vals_map(g, rows_ref, cols_ref, count_ref):
        last = jnp.maximum(count_ref[0] - 1, 0) // GROUP
        return (jnp.minimum(g, last), 0, 0)

    grid_spec = pltpu.PrefetchScalarGridSpec(
        num_scalar_prefetch=3,
        grid=(groups,),
        in_specs=[
            pl.BlockSpec((sections, blk, width), lambda g, *_: (0, 0, 0)),
            pl.BlockSpec((GROUP, blk, blk), vals_map),
        ],
        out_specs=pl.BlockSpec((rep_size, blk, width), lambda g, *_: (0, 0, 0)),
    )
    return pl.pallas_call(
        slot_kernel,
        grid_spec=grid_spec,
        out_shape=jax.ShapeDtypeStruct((rep_size, blk, width), jnp.float32),
        compiler_params=pltpu.CompilerParams(dimension_semantics=("arbitrary",)),
        cost_estimate=pl.CostEstimate(
            flops=2 * slot_total * blk * blk * width,
            bytes_accessed=vals.size * 2 + feats.size * 2 + rep_size * blk * width * 4,
            transcendentals=0,
        ),
    )(rows, cols, count, feats, vals)


def gather_over_row(x):
    row_size = lax.axis_size("row")
    x_size = row_size // 2
    i = lax.axis_index("row")
    lo = i // x_size
    xi = i % x_size
    other = lax.ppermute(x, "row", [(s, (s + x_size) % row_size) for s in range(row_size)])
    pair = jnp.where(lo == 0, jnp.stack([x, other]), jnp.stack([other, x]))
    out = jnp.zeros((x_size,) + pair.shape, x.dtype)
    out = lax.dynamic_update_index_in_dim(out, pair, xi, 0)
    for d in range(1, x_size):
        perm = [(s, (s // x_size) * x_size + (s % x_size + d) % x_size) for s in range(row_size)]
        got = lax.ppermute(pair, "row", perm)
        out = lax.dynamic_update_index_in_dim(out, got, (xi - d) % x_size, 0)
    return jnp.swapaxes(out, 0, 1).reshape((row_size,) + x.shape)


def reduce_over_rep(x):
    rep_size = x.shape[0]
    j = lax.axis_index("rep")
    c = j % 2
    y = (j // 2) % 4
    z = j // 8
    x = x.reshape((rep_size // 8, 4, 2) + x.shape[1:])
    keep = lax.dynamic_index_in_dim(x, c, 2, keepdims=False)
    send = lax.dynamic_index_in_dim(x, 1 - c, 2, keepdims=False)
    x = keep + lax.ppermute(send, "rep", [(i, i ^ 1) for i in range(rep_size)])
    acc = lax.dynamic_index_in_dim(x, y, 1, keepdims=False)
    for d in (1, 2, 3):
        send = lax.dynamic_index_in_dim(x, (y + d) % 4, 1, keepdims=False)
        perm = [(i, (i // 8) * 8 + (((i // 2) % 4 + d) % 4) * 2 + i % 2) for i in range(rep_size)]
        acc = acc + lax.ppermute(send, "rep", perm)
    x = acc
    z_size = x.shape[0]
    acc = lax.dynamic_index_in_dim(x, z, 0, keepdims=False)
    for d in range(1, z_size):
        send = lax.dynamic_index_in_dim(x, (z + d) % z_size, 0, keepdims=False)
        perm = [(i, (((i // 8) + d) % z_size) * 8 + i % 8) for i in range(rep_size)]
        acc = acc + lax.ppermute(send, "rep", perm)
    return acc


def per_device(features, block_values, block_rows, block_cols, block_count, weight, bias):
    block_size = features.shape[0]
    feature_width = features.shape[1]
    rep_size = lax.axis_size("rep")
    section_features = gather_over_row(features)
    device_index = lax.axis_index(("row", "rep"))
    live_count = lax.dynamic_slice_in_dim(block_count, device_index, 1, 0)
    partial_value = accumulate_slots(
        block_rows[0], block_cols[0], live_count, section_features, block_values, rep_size
    )
    summed = reduce_over_rep(partial_value)
    reduced = summed.astype(jnp.bfloat16)
    projected = jnp.dot(reduced, weight, preferred_element_type=jnp.float32) + bias
    return jax.nn.relu(projected).astype(jnp.bfloat16)


def solution(mesh):
    return jax.shard_map(
        per_device,
        mesh=mesh,
        in_specs=(
            P(("row", "rep"), None),
            P(("row", "rep"), None, None),
            P(("row", "rep"), None),
            P(("row", "rep"), None),
            P(),
            P(),
            P(),
        ),
        out_specs=P(("row", "rep"), None),
        check_vma=False,
    )
```

```python
import functools

import jax
import jax.numpy as jnp
from jax import lax
from jax.experimental import pallas as pl
from jax.experimental.pallas import tpu as pltpu
from jax.sharding import PartitionSpec as P

GROUP = 16


def slot_kernel(rows_ref, cols_ref, count_ref, feats_ref, vals_ref, out_ref):
    g = pl.program_id(0)
    live = count_ref[0]
    row_top = out_ref.shape[0] - 1
    col_top = feats_ref.shape[0] - 1

    @pl.when(g == 0)
    def _():
        out_ref[...] = jnp.zeros_like(out_ref)

    @pl.when(g * GROUP < live)
    def _():
        for s in range(GROUP):
            k = g * GROUP + s
            r = jnp.clip(rows_ref[k], 0, row_top)
            c = jnp.clip(cols_ref[k], 0, col_top)
            prod = jnp.dot(vals_ref[s], feats_ref[c], preferred_element_type=jnp.float32)
            out_ref[r] += jnp.where(k < live, prod, 0.0)


def accumulate_slots(rows, cols, count, feats, vals, rep_size):
    slot_total, blk, _ = vals.shape
    sections, _, width = feats.shape
    groups = slot_total // GROUP

    def vals_map(g, rows_ref, cols_ref, count_ref):
        last = jnp.maximum(count_ref[0] - 1, 0) // GROUP
        return (jnp.minimum(g, last), 0, 0)

    grid_spec = pltpu.PrefetchScalarGridSpec(
        num_scalar_prefetch=3,
        grid=(groups,),
        in_specs=[
            pl.BlockSpec((sections, blk, width), lambda g, *_: (0, 0, 0)),
            pl.BlockSpec((GROUP, blk, blk), vals_map),
        ],
        out_specs=pl.BlockSpec((rep_size, blk, width), lambda g, *_: (0, 0, 0)),
    )
    return pl.pallas_call(
        slot_kernel,
        grid_spec=grid_spec,
        out_shape=jax.ShapeDtypeStruct((rep_size, blk, width), jnp.float32),
        compiler_params=pltpu.CompilerParams(dimension_semantics=("arbitrary",)),
        cost_estimate=pl.CostEstimate(
            flops=2 * slot_total * blk * blk * width,
            bytes_accessed=vals.size * 2 + feats.size * 2 + rep_size * blk * width * 4,
            transcendentals=0,
        ),
    )(rows, cols, count, feats, vals)


def gather_over_row(x):
    row_size = lax.axis_size("row")
    x_size = row_size // 2
    i = lax.axis_index("row")
    lo = i // x_size
    xi = i % x_size
    other = lax.ppermute(x, "row", [(s, (s + x_size) % row_size) for s in range(row_size)])
    pair = jnp.where(lo == 0, jnp.stack([x, other]), jnp.stack([other, x]))
    out = jnp.zeros((x_size,) + pair.shape, x.dtype)
    out = lax.dynamic_update_index_in_dim(out, pair, xi, 0)
    for d in range(1, x_size):
        perm = [(s, (s // x_size) * x_size + (s % x_size + d) % x_size) for s in range(row_size)]
        got = lax.ppermute(pair, "row", perm)
        out = lax.dynamic_update_index_in_dim(out, got, (xi - d) % x_size, 0)
    return jnp.swapaxes(out, 0, 1).reshape((row_size,) + x.shape)


def reduce_over_rep(x):
    rep_size = x.shape[0]
    j = lax.axis_index("rep")
    c = j % 2
    y = (j // 2) % 4
    z = j // 8
    x = x.reshape((rep_size // 8, 4, 2) + x.shape[1:])
    keep = lax.dynamic_index_in_dim(x, c, 2, keepdims=False)
    send = lax.dynamic_index_in_dim(x, 1 - c, 2, keepdims=False)
    x = keep + lax.ppermute(send, "rep", [(i, i ^ 1) for i in range(rep_size)])
    acc = lax.dynamic_index_in_dim(x, y, 1, keepdims=False)
    for d in (1, 2, 3):
        send = lax.dynamic_index_in_dim(x, (y + d) % 4, 1, keepdims=False)
        perm = [(i, (i // 8) * 8 + (((i // 2) % 4 + d) % 4) * 2 + i % 2) for i in range(rep_size)]
        acc = acc + lax.ppermute(send, "rep", perm)
    x = acc
    z_size = x.shape[0]
    acc = lax.dynamic_index_in_dim(x, z, 0, keepdims=False)
    for d in range(1, z_size):
        send = lax.dynamic_index_in_dim(x, (z + d) % z_size, 0, keepdims=False)
        perm = [(i, (((i // 8) + d) % z_size) * 8 + i % 8) for i in range(rep_size)]
        acc = acc + lax.ppermute(send, "rep", perm)
    return acc


def per_device(features, block_values, block_rows, block_cols, block_count, weight, bias):
    block_size = features.shape[0]
    feature_width = features.shape[1]
    rep_size = lax.axis_size("rep")
    section_features = gather_over_row(features)
    device_index = lax.axis_index(("row", "rep"))
    live_count = lax.dynamic_slice_in_dim(block_count, device_index, 1, 0)
    partial_value = accumulate_slots(
        block_rows[0], block_cols[0], live_count, section_features, block_values, rep_size
    )
    summed = reduce_over_rep(partial_value)
    reduced = summed.astype(jnp.bfloat16)
    projected = jnp.dot(reduced, weight, preferred_element_type=jnp.float32) + bias
    return jax.nn.relu(projected).astype(jnp.bfloat16)


def solution(mesh):
    return jax.shard_map(
        per_device,
        mesh=mesh,
        in_specs=(
            P(("row", "rep"), None),
            P(("row", "rep"), None, None),
            P(("row", "rep"), None),
            P(("row", "rep"), None),
            P(),
            P(),
            P(),
        ),
        out_specs=P(("row", "rep"), None),
        check_vma=False,
    )
```

```python
import functools

import jax
import jax.numpy as jnp
from jax import lax
from jax.experimental import pallas as pl
from jax.experimental.pallas import tpu as pltpu
from jax.sharding import PartitionSpec as P

GROUP = 16
LINK = jnp.bfloat16


def slot_kernel(rows_ref, cols_ref, count_ref, feats_ref, vals_ref, out_ref):
    g = pl.program_id(0)
    live = count_ref[0]
    row_top = out_ref.shape[0] - 1
    col_top = feats_ref.shape[0] - 1

    @pl.when(g == 0)
    def _():
        out_ref[...] = jnp.zeros_like(out_ref)

    @pl.when(g * GROUP < live)
    def _():
        for s in range(GROUP):
            k = g * GROUP + s
            r = jnp.clip(rows_ref[k], 0, row_top)
            c = jnp.clip(cols_ref[k], 0, col_top)
            prod = jnp.dot(vals_ref[s], feats_ref[c], preferred_element_type=jnp.float32)
            out_ref[r] += jnp.where(k < live, prod, 0.0)


def accumulate_slots(rows, cols, count, feats, vals, rep_size):
    slot_total, blk, _ = vals.shape
    sections, _, width = feats.shape
    groups = slot_total // GROUP

    def vals_map(g, rows_ref, cols_ref, count_ref):
        last = jnp.maximum(count_ref[0] - 1, 0) // GROUP
        return (jnp.minimum(g, last), 0, 0)

    grid_spec = pltpu.PrefetchScalarGridSpec(
        num_scalar_prefetch=3,
        grid=(groups,),
        in_specs=[
            pl.BlockSpec((sections, blk, width), lambda g, *_: (0, 0, 0)),
            pl.BlockSpec((GROUP, blk, blk), vals_map),
        ],
        out_specs=pl.BlockSpec((rep_size, blk, width), lambda g, *_: (0, 0, 0)),
    )
    return pl.pallas_call(
        slot_kernel,
        grid_spec=grid_spec,
        out_shape=jax.ShapeDtypeStruct((rep_size, blk, width), jnp.float32),
        compiler_params=pltpu.CompilerParams(dimension_semantics=("arbitrary",)),
        cost_estimate=pl.CostEstimate(
            flops=2 * slot_total * blk * blk * width,
            bytes_accessed=vals.size * 2 + feats.size * 2 + rep_size * blk * width * 4,
            transcendentals=0,
        ),
    )(rows, cols, count, feats, vals)


def gather_over_row(x):
    row_size = lax.axis_size("row")
    x_size = row_size // 2
    i = lax.axis_index("row")
    lo = i // x_size
    xi = i % x_size
    other = lax.ppermute(x, "row", [(s, (s + x_size) % row_size) for s in range(row_size)])
    pair = jnp.where(lo == 0, jnp.stack([x, other]), jnp.stack([other, x]))
    out = jnp.zeros((x_size,) + pair.shape, x.dtype)
    out = lax.dynamic_update_index_in_dim(out, pair, xi, 0)
    for d in range(1, x_size):
        perm = [(s, (s // x_size) * x_size + (s % x_size + d) % x_size) for s in range(row_size)]
        got = lax.ppermute(pair, "row", perm)
        out = lax.dynamic_update_index_in_dim(out, got, (xi - d) % x_size, 0)
    return jnp.swapaxes(out, 0, 1).reshape((row_size,) + x.shape)


def reduce_over_rep(x):
    rep_size = x.shape[0]
    j = lax.axis_index("rep")
    c = j % 2
    y = (j // 2) % 4
    z = j // 8
    x = x.reshape((rep_size // 8, 4, 2) + x.shape[1:])
    keep = lax.dynamic_index_in_dim(x, c, 2, keepdims=False)
    send = lax.dynamic_index_in_dim(x, 1 - c, 2, keepdims=False)
    x = keep + lax.ppermute(send, "rep", [(i, i ^ 1) for i in range(rep_size)])
    acc = lax.dynamic_index_in_dim(x, y, 1, keepdims=False)
    for d in (1, 2, 3):
        send = lax.dynamic_index_in_dim(x, (y + d) % 4, 1, keepdims=False)
        perm = [(i, (i // 8) * 8 + (((i // 2) % 4 + d) % 4) * 2 + i % 2) for i in range(rep_size)]
        acc = acc + lax.ppermute(send.astype(LINK), "rep", perm).astype(jnp.float32)
    x = acc
    z_size = x.shape[0]
    acc = lax.dynamic_index_in_dim(x, z, 0, keepdims=False)
    for d in range(1, z_size):
        send = lax.dynamic_index_in_dim(x, (z + d) % z_size, 0, keepdims=False)
        perm = [(i, (((i // 8) + d) % z_size) * 8 + i % 8) for i in range(rep_size)]
        acc = acc + lax.ppermute(send.astype(LINK), "rep", perm).astype(jnp.float32)
    return acc


def per_device(features, block_values, block_rows, block_cols, block_count, weight, bias):
    block_size = features.shape[0]
    feature_width = features.shape[1]
    rep_size = lax.axis_size("rep")
    section_features = gather_over_row(features)
    device_index = lax.axis_index(("row", "rep"))
    live_count = lax.dynamic_slice_in_dim(block_count, device_index, 1, 0)
    partial_value = accumulate_slots(
        block_rows[0], block_cols[0], live_count, section_features, block_values, rep_size
    )
    summed = reduce_over_rep(partial_value)
    reduced = summed.astype(jnp.bfloat16)
    projected = jnp.dot(reduced, weight, preferred_element_type=jnp.float32) + bias
    return jax.nn.relu(projected).astype(jnp.bfloat16)


def solution(mesh):
    return jax.shard_map(
        per_device,
        mesh=mesh,
        in_specs=(
            P(("row", "rep"), None),
            P(("row", "rep"), None, None),
            P(("row", "rep"), None),
            P(("row", "rep"), None),
            P(),
            P(),
            P(),
        ),
        out_specs=P(("row", "rep"), None),
        check_vma=False,
    )
```

```python
import functools

import jax
import jax.numpy as jnp
from jax import lax
from jax.experimental import pallas as pl
from jax.experimental.pallas import tpu as pltpu
from jax.sharding import PartitionSpec as P

GROUP = 16


def slot_kernel(rows_ref, cols_ref, meta_ref, feats_ref, vals_ref, out_ref):
    g = pl.program_id(0)
    live = meta_ref[0]
    lo = meta_ref[1]
    xi = meta_ref[2]
    core = meta_ref[3]
    x_size = feats_ref.shape[0] // 2
    half_rows = out_ref.shape[1]

    @pl.when(g == 0)
    def _():
        out_ref[...] = jnp.zeros_like(out_ref)

    @pl.when(g * GROUP < live)
    def _():
        for s in range(GROUP):
            k = g * GROUP + s
            r = jnp.clip(rows_ref[k], 0, 2 * half_rows - 1)
            c = jnp.clip(cols_ref[k], 0, 2 * x_size - 1)
            spot = ((xi - c % x_size) % x_size) * 2 + ((c // x_size) ^ lo)
            prod = jnp.dot(vals_ref[s], feats_ref[spot], preferred_element_type=jnp.float32)
            side = jnp.where(r % 2 == core, 0, 1)
            out_ref[side, r // 2] += jnp.where(k < live, prod, 0.0)


def accumulate_slots(rows, cols, meta, feats, vals, rep_size):
    slot_total, blk, _ = vals.shape
    sections, _, width = feats.shape
    groups = slot_total // GROUP

    def vals_map(g, rows_ref, cols_ref, meta_ref):
        last = jnp.maximum(meta_ref[0] - 1, 0) // GROUP
        return (jnp.minimum(g, last), 0, 0)

    grid_spec = pltpu.PrefetchScalarGridSpec(
        num_scalar_prefetch=3,
        grid=(groups,),
        in_specs=[
            pl.BlockSpec((sections, blk, width), lambda g, *_: (0, 0, 0)),
            pl.BlockSpec((GROUP, blk, blk), vals_map),
        ],
        out_specs=pl.BlockSpec((2, rep_size // 2, blk, width), lambda g, *_: (0, 0, 0, 0)),
    )
    return pl.pallas_call(
        slot_kernel,
        grid_spec=grid_spec,
        out_shape=jax.ShapeDtypeStruct((2, rep_size // 2, blk, width), jnp.float32),
        compiler_params=pltpu.CompilerParams(dimension_semantics=("arbitrary",)),
        cost_estimate=pl.CostEstimate(
            flops=2 * slot_total * blk * blk * width,
            bytes_accessed=vals.size * 2 + feats.size * 2 + rep_size * blk * width * 4,
            transcendentals=0,
        ),
    )(rows, cols, meta, feats, vals)


def gather_over_row(x):
    row_size = lax.axis_size("row")
    x_size = row_size // 2
    other = lax.ppermute(x, "row", [(s, (s + x_size) % row_size) for s in range(row_size)])
    pair = jnp.stack([x, other])
    parts = [pair]
    for d in range(1, x_size):
        perm = [(s, (s // x_size) * x_size + (s % x_size + d) % x_size) for s in range(row_size)]
        parts.append(lax.ppermute(pair, "row", perm))
    return jnp.concatenate(parts, axis=0)


def reduce_over_rep(x):
    rep_size = 2 * x.shape[1]
    j = lax.axis_index("rep")
    c = j % 2
    y = (j // 2) % 4
    z = j // 8
    shape = (rep_size // 8, 4) + x.shape[2:]
    x = x[0].reshape(shape) + lax.ppermute(
        x[1].reshape(shape), "rep", [(i, i ^ 1) for i in range(rep_size)]
    )
    acc = lax.dynamic_index_in_dim(x, y, 1, keepdims=False)
    for d in (1, 2, 3):
        send = lax.dynamic_index_in_dim(x, (y + d) % 4, 1, keepdims=False)
        perm = [(i, (i // 8) * 8 + (((i // 2) % 4 + d) % 4) * 2 + i % 2) for i in range(rep_size)]
        acc = acc + lax.ppermute(send, "rep", perm)
    x = acc
    z_size = x.shape[0]
    acc = lax.dynamic_index_in_dim(x, z, 0, keepdims=False)
    for d in range(1, z_size):
        send = lax.dynamic_index_in_dim(x, (z + d) % z_size, 0, keepdims=False)
        perm = [(i, (((i // 8) + d) % z_size) * 8 + i % 8) for i in range(rep_size)]
        acc = acc + lax.ppermute(send, "rep", perm)
    return acc


def per_device(features, block_values, block_rows, block_cols, block_count, weight, bias):
    block_size = features.shape[0]
    feature_width = features.shape[1]
    rep_size = lax.axis_size("rep")
    section_features = gather_over_row(features)
    device_index = lax.axis_index(("row", "rep"))
    row_index = lax.axis_index("row")
    x_size = lax.axis_size("row") // 2
    meta = jnp.stack(
        [
            block_count[device_index],
            row_index // x_size,
            row_index % x_size,
            lax.axis_index("rep") % 2,
        ]
    ).astype(jnp.int32)
    partial_value = accumulate_slots(
        block_rows[0], block_cols[0], meta, section_features, block_values, rep_size
    )
    summed = reduce_over_rep(partial_value)
    reduced = summed.astype(jnp.bfloat16)
    projected = jnp.dot(reduced, weight, preferred_element_type=jnp.float32) + bias
    return jax.nn.relu(projected).astype(jnp.bfloat16)


def solution(mesh):
    return jax.shard_map(
        per_device,
        mesh=mesh,
        in_specs=(
            P(("row", "rep"), None),
            P(("row", "rep"), None, None),
            P(("row", "rep"), None),
            P(("row", "rep"), None),
            P(),
            P(),
            P(),
        ),
        out_specs=P(("row", "rep"), None),
        check_vma=False,
    )
```

```python
import functools

import jax
import jax.numpy as jnp
from jax import lax
from jax.experimental import pallas as pl
from jax.experimental.pallas import tpu as pltpu
from jax.sharding import PartitionSpec as P

GROUP = 64


def slot_kernel(rows_ref, cols_ref, count_ref, feats_ref, vals_ref, out_ref):
    g = pl.program_id(0)
    live = count_ref[0]
    row_top = out_ref.shape[0] - 1
    col_top = feats_ref.shape[0] - 1

    @pl.when(g == 0)
    def _():
        out_ref[...] = jnp.zeros_like(out_ref)

    @pl.when(g * GROUP < live)
    def _():
        for s in range(GROUP):
            k = g * GROUP + s
            r = jnp.clip(rows_ref[k], 0, row_top)
            c = jnp.clip(cols_ref[k], 0, col_top)
            prod = jnp.dot(vals_ref[s], feats_ref[c], preferred_element_type=jnp.float32)
            out_ref[r] += jnp.where(k < live, prod, 0.0)


def accumulate_slots(rows, cols, count, feats, vals, rep_size):
    slot_total, blk, _ = vals.shape
    sections, _, width = feats.shape
    groups = slot_total // GROUP

    def vals_map(g, rows_ref, cols_ref, count_ref):
        last = jnp.maximum(count_ref[0] - 1, 0) // GROUP
        return (jnp.minimum(g, last), 0, 0)

    grid_spec = pltpu.PrefetchScalarGridSpec(
        num_scalar_prefetch=3,
        grid=(groups,),
        in_specs=[
            pl.BlockSpec((sections, blk, width), lambda g, *_: (0, 0, 0)),
            pl.BlockSpec((GROUP, blk, blk), vals_map),
        ],
        out_specs=pl.BlockSpec((rep_size, blk, width), lambda g, *_: (0, 0, 0)),
    )
    return pl.pallas_call(
        slot_kernel,
        grid_spec=grid_spec,
        out_shape=jax.ShapeDtypeStruct((rep_size, blk, width), jnp.float32),
        compiler_params=pltpu.CompilerParams(dimension_semantics=("arbitrary",)),
        cost_estimate=pl.CostEstimate(
            flops=2 * slot_total * blk * blk * width,
            bytes_accessed=vals.size * 2 + feats.size * 2 + rep_size * blk * width * 4,
            transcendentals=0,
        ),
    )(rows, cols, count, feats, vals)


def gather_over_row(x):
    row_size = lax.axis_size("row")
    x_size = row_size // 2
    i = lax.axis_index("row")
    lo = i // x_size
    xi = i % x_size
    other = lax.ppermute(x, "row", [(s, (s + x_size) % row_size) for s in range(row_size)])
    pair = jnp.where(lo == 0, jnp.stack([x, other]), jnp.stack([other, x]))
    out = jnp.zeros((x_size,) + pair.shape, x.dtype)
    out = lax.dynamic_update_index_in_dim(out, pair, xi, 0)
    for d in range(1, x_size):
        perm = [(s, (s // x_size) * x_size + (s % x_size + d) % x_size) for s in range(row_size)]
        got = lax.ppermute(pair, "row", perm)
        out = lax.dynamic_update_index_in_dim(out, got, (xi - d) % x_size, 0)
    return jnp.swapaxes(out, 0, 1).reshape((row_size,) + x.shape)


def reduce_over_rep(x):
    rep_size = x.shape[0]
    j = lax.axis_index("rep")
    c = j % 2
    y = (j // 2) % 4
    z = j // 8
    x = x.reshape((rep_size // 8, 4, 2) + x.shape[1:])
    keep = lax.dynamic_index_in_dim(x, c, 2, keepdims=False)
    send = lax.dynamic_index_in_dim(x, 1 - c, 2, keepdims=False)
    x = keep + lax.ppermute(send, "rep", [(i, i ^ 1) for i in range(rep_size)])
    acc = lax.dynamic_index_in_dim(x, y, 1, keepdims=False)
    for d in (1, 2, 3):
        send = lax.dynamic_index_in_dim(x, (y + d) % 4, 1, keepdims=False)
        perm = [(i, (i // 8) * 8 + (((i // 2) % 4 + d) % 4) * 2 + i % 2) for i in range(rep_size)]
        acc = acc + lax.ppermute(send, "rep", perm)
    x = acc
    z_size = x.shape[0]
    acc = lax.dynamic_index_in_dim(x, z, 0, keepdims=False)
    for d in range(1, z_size):
        send = lax.dynamic_index_in_dim(x, (z + d) % z_size, 0, keepdims=False)
        perm = [(i, (((i // 8) + d) % z_size) * 8 + i % 8) for i in range(rep_size)]
        acc = acc + lax.ppermute(send, "rep", perm)
    return acc


def per_device(features, block_values, block_rows, block_cols, block_count, weight, bias):
    block_size = features.shape[0]
    feature_width = features.shape[1]
    rep_size = lax.axis_size("rep")
    section_features = gather_over_row(features)
    device_index = lax.axis_index(("row", "rep"))
    live_count = lax.dynamic_slice_in_dim(block_count, device_index, 1, 0)
    partial_value = accumulate_slots(
        block_rows[0], block_cols[0], live_count, section_features, block_values, rep_size
    )
    summed = reduce_over_rep(partial_value)
    reduced = summed.astype(jnp.bfloat16)
    projected = jnp.dot(reduced, weight, preferred_element_type=jnp.float32) + bias
    return jax.nn.relu(projected).astype(jnp.bfloat16)


def solution(mesh):
    return jax.shard_map(
        per_device,
        mesh=mesh,
        in_specs=(
            P(("row", "rep"), None),
            P(("row", "rep"), None, None),
            P(("row", "rep"), None),
            P(("row", "rep"), None),
            P(),
            P(),
            P(),
        ),
        out_specs=P(("row", "rep"), None),
        check_vma=False,
    )
```

```python
import functools

import jax
import jax.numpy as jnp
from jax import lax
from jax.experimental import pallas as pl
from jax.experimental.pallas import tpu as pltpu
from jax.sharding import PartitionSpec as P

GROUP = 64


def slot_kernel(rows_ref, cols_ref, count_ref, feats_ref, vals_ref, keep_ref, send_ref, acc_ref):
    g = pl.program_id(0)
    live = count_ref[0]
    row_index = lax.axis_index("row")
    core = lax.axis_index("rep") % 2
    x_size = feats_ref.shape[0] // 2
    lo = row_index // x_size
    xi = row_index % x_size
    row_top = acc_ref.shape[0] - 1

    @pl.when(g == 0)
    def _():
        acc_ref[...] = jnp.zeros_like(acc_ref)

    @pl.when(g * GROUP < live)
    def _():
        for s in range(GROUP):
            k = g * GROUP + s
            r = jnp.clip(rows_ref[k], 0, row_top)
            c = jnp.clip(cols_ref[k], 0, 2 * x_size - 1)
            spot = ((xi - c % x_size) % x_size) * 2 + ((c // x_size) ^ lo)
            prod = jnp.dot(vals_ref[s], feats_ref[spot], preferred_element_type=jnp.float32)
            acc_ref[r] += jnp.where(k < live, prod, 0.0)

    @pl.when(g == pl.num_programs(0) - 1)
    def _():
        for t in range(keep_ref.shape[0]):
            keep_ref[t] = acc_ref[2 * t + core]
            send_ref[t] = acc_ref[2 * t + 1 - core]


def accumulate_slots(rows, cols, count, feats, vals, rep_size):
    slot_total, blk, _ = vals.shape
    sections, _, width = feats.shape
    groups = slot_total // GROUP

    def vals_map(g, rows_ref, cols_ref, count_ref):
        last = jnp.maximum(count_ref[0] - 1, 0) // GROUP
        return (jnp.minimum(g, last), 0, 0)

    half = jax.ShapeDtypeStruct((rep_size // 2, blk, width), jnp.float32)
    half_spec = pl.BlockSpec((rep_size // 2, blk, width), lambda g, *_: (0, 0, 0))
    grid_spec = pltpu.PrefetchScalarGridSpec(
        num_scalar_prefetch=3,
        grid=(groups,),
        in_specs=[
            pl.BlockSpec((sections, blk, width), lambda g, *_: (0, 0, 0)),
            pl.BlockSpec((GROUP, blk, blk), vals_map),
        ],
        out_specs=[half_spec, half_spec],
        scratch_shapes=[pltpu.VMEM((rep_size, blk, width), jnp.float32)],
    )
    return pl.pallas_call(
        slot_kernel,
        grid_spec=grid_spec,
        out_shape=[half, half],
        compiler_params=pltpu.CompilerParams(dimension_semantics=("arbitrary",)),
        cost_estimate=pl.CostEstimate(
            flops=2 * slot_total * blk * blk * width,
            bytes_accessed=vals.size * 2 + feats.size * 2 + rep_size * blk * width * 4,
            transcendentals=0,
        ),
    )(rows, cols, count, feats, vals)


def gather_over_row(x):
    row_size = lax.axis_size("row")
    x_size = row_size // 2
    other = lax.ppermute(x, "row", [(s, (s + x_size) % row_size) for s in range(row_size)])
    pair = jnp.stack([x, other])
    parts = [pair]
    for d in range(1, x_size):
        perm = [(s, (s // x_size) * x_size + (s % x_size + d) % x_size) for s in range(row_size)]
        parts.append(lax.ppermute(pair, "row", perm))
    return jnp.concatenate(parts, axis=0)


def reduce_over_rep(keep, send):
    rep_size = 2 * keep.shape[0]
    j = lax.axis_index("rep")
    y = (j // 2) % 4
    z = j // 8
    shape = (rep_size // 8, 4) + keep.shape[1:]
    x = keep.reshape(shape) + lax.ppermute(
        send.reshape(shape), "rep", [(i, i ^ 1) for i in range(rep_size)]
    )
    acc = lax.dynamic_index_in_dim(x, y, 1, keepdims=False)
    for d in (1, 2, 3):
        send = lax.dynamic_index_in_dim(x, (y + d) % 4, 1, keepdims=False)
        perm = [(i, (i // 8) * 8 + (((i // 2) % 4 + d) % 4) * 2 + i % 2) for i in range(rep_size)]
        acc = acc + lax.ppermute(send, "rep", perm)
    x = acc
    z_size = x.shape[0]
    acc = lax.dynamic_index_in_dim(x, z, 0, keepdims=False)
    for d in range(1, z_size):
        send = lax.dynamic_index_in_dim(x, (z + d) % z_size, 0, keepdims=False)
        perm = [(i, (((i // 8) + d) % z_size) * 8 + i % 8) for i in range(rep_size)]
        acc = acc + lax.ppermute(send, "rep", perm)
    return acc


def per_device(features, block_values, block_rows, block_cols, block_count, weight, bias):
    block_size = features.shape[0]
    feature_width = features.shape[1]
    rep_size = lax.axis_size("rep")
    section_features = gather_over_row(features)
    device_index = lax.axis_index(("row", "rep"))
    live_count = lax.dynamic_slice_in_dim(block_count, device_index, 1, 0)
    keep, send = accumulate_slots(
        block_rows[0], block_cols[0], live_count, section_features, block_values, rep_size
    )
    summed = reduce_over_rep(keep, send)
    reduced = summed.astype(jnp.bfloat16)
    projected = jnp.dot(reduced, weight, preferred_element_type=jnp.float32) + bias
    return jax.nn.relu(projected).astype(jnp.bfloat16)


def solution(mesh):
    return jax.shard_map(
        per_device,
        mesh=mesh,
        in_specs=(
            P(("row", "rep"), None),
            P(("row", "rep"), None, None),
            P(("row", "rep"), None),
            P(("row", "rep"), None),
            P(),
            P(),
            P(),
        ),
        out_specs=P(("row", "rep"), None),
        check_vma=False,
    )
```

```python
import functools

import jax
import jax.numpy as jnp
from jax import lax
from jax.experimental import pallas as pl
from jax.experimental.pallas import tpu as pltpu
from jax.sharding import PartitionSpec as P

GROUP = 64


def slot_kernel(rows_ref, cols_ref, count_ref, feats_ref, vals_ref, keep_ref, send_ref, acc_ref):
    g = pl.program_id(0)
    live = count_ref[0]
    row_index = lax.axis_index("row")
    core = lax.axis_index("rep") % 2
    x_size = feats_ref.shape[0] // 2
    lo = row_index // x_size
    xi = row_index % x_size
    row_top = acc_ref.shape[0] - 1

    @pl.when(g == 0)
    def _():
        acc_ref[...] = jnp.zeros_like(acc_ref)

    @pl.when(g * GROUP < live)
    def _():
        for s in range(GROUP):
            k = g * GROUP + s
            r = jnp.clip(rows_ref[k], 0, row_top)
            c = jnp.clip(cols_ref[k], 0, 2 * x_size - 1)
            spot = ((xi - c % x_size) % x_size) * 2 + ((c // x_size) ^ lo)
            prod = jnp.dot(vals_ref[s], feats_ref[spot], preferred_element_type=jnp.float32)
            acc_ref[r] += jnp.where(k < live, prod, 0.0)

    @pl.when(g == pl.num_programs(0) - 1)
    def _():
        for t in range(keep_ref.shape[0]):
            keep_ref[t] = acc_ref[2 * t + core]
            send_ref[t] = acc_ref[2 * t + 1 - core]


def accumulate_slots(rows, cols, count, feats, vals, rep_size):
    slot_total, blk, _ = vals.shape
    sections, _, width = feats.shape
    groups = slot_total // GROUP

    def vals_map(g, rows_ref, cols_ref, count_ref):
        last = jnp.maximum(count_ref[0] - 1, 0) // GROUP
        return (jnp.minimum(g, last), 0, 0)

    half = jax.ShapeDtypeStruct((rep_size // 2, blk, width), jnp.float32)
    half_spec = pl.BlockSpec((rep_size // 2, blk, width), lambda g, *_: (0, 0, 0))
    grid_spec = pltpu.PrefetchScalarGridSpec(
        num_scalar_prefetch=3,
        grid=(groups,),
        in_specs=[
            pl.BlockSpec((sections, blk, width), lambda g, *_: (0, 0, 0)),
            pl.BlockSpec((GROUP, blk, blk), vals_map),
        ],
        out_specs=[half_spec, half_spec],
        scratch_shapes=[pltpu.VMEM((rep_size, blk, width), jnp.float32)],
    )
    return pl.pallas_call(
        slot_kernel,
        grid_spec=grid_spec,
        out_shape=[half, half],
        compiler_params=pltpu.CompilerParams(dimension_semantics=("arbitrary",)),
        cost_estimate=pl.CostEstimate(
            flops=2 * slot_total * blk * blk * width,
            bytes_accessed=vals.size * 2 + feats.size * 2 + rep_size * blk * width * 4,
            transcendentals=0,
        ),
    )(rows, cols, count, feats, vals)


def gather_over_row(x):
    row_size = lax.axis_size("row")
    x_size = row_size // 2
    other = lax.ppermute(x, "row", [(s, (s + x_size) % row_size) for s in range(row_size)])
    pair = jnp.stack([x, other])
    parts = [pair]
    for d in range(1, x_size):
        perm = [(s, (s // x_size) * x_size + (s % x_size + d) % x_size) for s in range(row_size)]
        parts.append(lax.ppermute(pair, "row", perm))
    return jnp.concatenate(parts, axis=0)


def y_pairs(rep_size, d):
    return [(i, (i // 8) * 8 + (((i // 2) % 4 + d) % 4) * 2 + i % 2) for i in range(rep_size)]


def z_pairs(rep_size, z_size, d):
    return [(i, (((i // 8) + d) % z_size) * 8 + i % 8) for i in range(rep_size)]


def reduce_over_rep(keep, send):
    rep_size = 2 * keep.shape[0]
    z_size = rep_size // 8
    j = lax.axis_index("rep")
    y = (j // 2) % 4
    z = j // 8
    shape = (z_size, 4) + keep.shape[1:]
    x = keep.reshape(shape) + lax.ppermute(
        send.reshape(shape), "rep", [(i, i ^ 1) for i in range(rep_size)]
    )
    early = [d for d in range(1, z_size) if d < z_size - 1]
    late = [0] + [d for d in range(1, z_size) if d not in early]
    blocks = {}
    for shifts in (early, late):
        part = jnp.stack(
            [lax.dynamic_index_in_dim(x, (z + d) % z_size, 0, keepdims=False) for d in shifts]
        )
        acc = lax.dynamic_index_in_dim(part, y, 1, keepdims=False)
        for dy in (1, 2, 3):
            sent = lax.dynamic_index_in_dim(part, (y + dy) % 4, 1, keepdims=False)
            acc = acc + lax.ppermute(sent, "rep", y_pairs(rep_size, dy))
        for n, d in enumerate(shifts):
            blocks[d] = acc[n]
    out = blocks[0]
    for d in range(1, z_size):
        out = out + lax.ppermute(blocks[d], "rep", z_pairs(rep_size, z_size, d))
    return out


def per_device(features, block_values, block_rows, block_cols, block_count, weight, bias):
    block_size = features.shape[0]
    feature_width = features.shape[1]
    rep_size = lax.axis_size("rep")
    section_features = gather_over_row(features)
    device_index = lax.axis_index(("row", "rep"))
    live_count = lax.dynamic_slice_in_dim(block_count, device_index, 1, 0)
    keep, send = accumulate_slots(
        block_rows[0], block_cols[0], live_count, section_features, block_values, rep_size
    )
    summed = reduce_over_rep(keep, send)
    reduced = summed.astype(jnp.bfloat16)
    projected = jnp.dot(reduced, weight, preferred_element_type=jnp.float32) + bias
    return jax.nn.relu(projected).astype(jnp.bfloat16)


def solution(mesh):
    return jax.shard_map(
        per_device,
        mesh=mesh,
        in_specs=(
            P(("row", "rep"), None),
            P(("row", "rep"), None, None),
            P(("row", "rep"), None),
            P(("row", "rep"), None),
            P(),
            P(),
            P(),
        ),
        out_specs=P(("row", "rep"), None),
        check_vma=False,
    )
```

```python
import jax
import jax.numpy as jnp
from jax import lax
from jax.experimental import pallas as pl
from jax.experimental.pallas import tpu as pltpu
from jax.sharding import PartitionSpec as P


GROUP = 64


def slot_kernel(rows_ref, cols_ref, count_ref, feats_ref, vals_ref, keep_ref, send_ref, acc_ref):
    g = pl.program_id(0)
    live = count_ref[0]
    row_index = lax.axis_index("row")
    core = lax.axis_index("rep") % 2
    x_size = feats_ref.shape[0] // 2
    lo = row_index // x_size
    xi = row_index % x_size
    row_top = acc_ref.shape[0] - 1

    @pl.when(g == 0)
    def _():
        acc_ref[...] = jnp.zeros_like(acc_ref)

    @pl.when(g * GROUP < live)
    def _():
        for s in range(GROUP):
            k = g * GROUP + s
            r = jnp.clip(rows_ref[k], 0, row_top)
            c = jnp.clip(cols_ref[k], 0, 2 * x_size - 1)
            spot = ((xi - c % x_size) % x_size) * 2 + ((c // x_size) ^ lo)
            prod = jnp.dot(vals_ref[s], feats_ref[spot], preferred_element_type=jnp.float32)
            acc_ref[r] += jnp.where(k < live, prod, 0.0)

    @pl.when(g == pl.num_programs(0) - 1)
    def _():
        for t in range(keep_ref.shape[0]):
            keep_ref[t] = acc_ref[2 * t + core]
            send_ref[t] = acc_ref[2 * t + 1 - core]


def accumulate_slots(rows, cols, count, feats, vals, rep_size):
    slot_total, blk, _ = vals.shape
    sections, _, width = feats.shape
    groups = slot_total // GROUP

    def vals_map(g, rows_ref, cols_ref, count_ref):
        last = jnp.maximum(count_ref[0] - 1, 0) // GROUP
        return (jnp.minimum(g, last), 0, 0)

    half = jax.ShapeDtypeStruct((rep_size // 2, blk, width), jnp.float32)
    half_spec = pl.BlockSpec((rep_size // 2, blk, width), lambda g, *_: (0, 0, 0))
    grid_spec = pltpu.PrefetchScalarGridSpec(
        num_scalar_prefetch=3,
        grid=(groups,),
        in_specs=[
            pl.BlockSpec((sections, blk, width), lambda g, *_: (0, 0, 0)),
            pl.BlockSpec((GROUP, blk, blk), vals_map),
        ],
        out_specs=[half_spec, half_spec],
        scratch_shapes=[pltpu.VMEM((rep_size, blk, width), jnp.float32)],
    )
    return pl.pallas_call(
        slot_kernel,
        grid_spec=grid_spec,
        out_shape=[half, half],
        compiler_params=pltpu.CompilerParams(dimension_semantics=("arbitrary",)),
        cost_estimate=pl.CostEstimate(
            flops=2 * slot_total * blk * blk * width,
            bytes_accessed=vals.size * 2 + feats.size * 2 + rep_size * blk * width * 4,
            transcendentals=0,
        ),
    )(rows, cols, count, feats, vals)


def gather_over_row(x):
    row_size = lax.axis_size("row")
    x_size = row_size // 2
    other = lax.ppermute(x, "row", [(s, (s + x_size) % row_size) for s in range(row_size)])
    pair = jnp.stack([x, other])
    parts = [pair]
    for d in range(1, x_size):
        perm = [(s, (s // x_size) * x_size + (s % x_size + d) % x_size) for s in range(row_size)]
        parts.append(lax.ppermute(pair, "row", perm))
    return jnp.concatenate(parts, axis=0)


def y_pairs(rep_size, d):
    return [(i, (i // 8) * 8 + (((i // 2) % 4 + d) % 4) * 2 + i % 2) for i in range(rep_size)]


def z_pairs(rep_size, z_size, d):
    return [(i, (((i // 8) + d) % z_size) * 8 + i % 8) for i in range(rep_size)]


def reduce_over_rep(keep, send):
    rep_size = 2 * keep.shape[0]
    z_size = rep_size // 8
    j = lax.axis_index("rep")
    y = (j // 2) % 4
    z = j // 8
    shape = (z_size, 4) + keep.shape[1:]
    x = keep.reshape(shape) + lax.ppermute(
        send.reshape(shape), "rep", [(i, i ^ 1) for i in range(rep_size)]
    )
    early = [d for d in range(1, z_size) if d < z_size - 1]
    late = [0] + [d for d in range(1, z_size) if d not in early]
    blocks = {}
    for shifts in (early, late):
        part = jnp.stack(
            [lax.dynamic_index_in_dim(x, (z + d) % z_size, 0, keepdims=False) for d in shifts]
        )
        acc = lax.dynamic_index_in_dim(part, y, 1, keepdims=False)
        got = [
            lax.ppermute(
                lax.dynamic_index_in_dim(part, (y + dy) % 4, 1, keepdims=False),
                "rep",
                y_pairs(rep_size, dy),
            )
            for dy in (1, 2, 3)
        ]
        for piece in got:
            acc = acc + piece
        for n, d in enumerate(shifts):
            blocks[d] = acc[n]
    out = blocks[0]
    for d in range(1, z_size):
        out = out + lax.ppermute(blocks[d], "rep", z_pairs(rep_size, z_size, d))
    return out


def layer(features, block_values, block_rows, block_cols, block_count, weight, bias):
    rep_size = lax.axis_size("rep")
    section_features = gather_over_row(features)
    device_index = lax.axis_index(("row", "rep"))
    live_count = lax.dynamic_slice_in_dim(block_count, device_index, 1, 0)
    keep, send = accumulate_slots(
        block_rows[0], block_cols[0], live_count, section_features, block_values, rep_size
    )
    summed = reduce_over_rep(keep, send)
    reduced = summed.astype(jnp.bfloat16)
    projected = jnp.dot(reduced, weight, preferred_element_type=jnp.float32) + bias
    return jax.nn.relu(projected).astype(jnp.bfloat16)


def solution(mesh):
    return jax.shard_map(
        layer,
        mesh=mesh,
        in_specs=(
            P(("row", "rep"), None),
            P(("row", "rep"), None, None),
            P(("row", "rep"), None),
            P(("row", "rep"), None),
            P(),
            P(),
            P(),
        ),
        out_specs=P(("row", "rep"), None),
        check_vma=False,
    )
```

```python
import jax
import jax.numpy as jnp
from jax import lax
from jax.experimental import pallas as pl
from jax.experimental.pallas import tpu as pltpu
from jax.sharding import PartitionSpec as P


GROUP = 64


def slot_kernel(rows_ref, cols_ref, count_ref, feats_ref, vals_ref, keep_ref, send_ref, acc_ref):
    g = pl.program_id(0)
    live = count_ref[0]
    row_index = lax.axis_index("row")
    core = lax.axis_index("rep") % 2
    x_size = feats_ref.shape[0] // 2
    lo = row_index // x_size
    xi = row_index % x_size
    row_top = acc_ref.shape[0] - 1

    @pl.when(g == 0)
    def _():
        acc_ref[...] = jnp.zeros_like(acc_ref)

    @pl.when(g * GROUP < live)
    def _():
        for s in range(GROUP):
            k = g * GROUP + s
            r = jnp.clip(rows_ref[k], 0, row_top)
            c = jnp.clip(cols_ref[k], 0, 2 * x_size - 1)
            spot = ((xi - c % x_size) % x_size) * 2 + ((c // x_size) ^ lo)
            prod = jnp.dot(vals_ref[s], feats_ref[spot], preferred_element_type=jnp.float32)
            acc_ref[r] += jnp.where(k < live, prod, 0.0)

    @pl.when(g == pl.num_programs(0) - 1)
    def _():
        for t in range(keep_ref.shape[0]):
            keep_ref[t] = acc_ref[2 * t + core]
            send_ref[t] = acc_ref[2 * t + 1 - core]


def accumulate_slots(rows, cols, count, feats, vals, rep_size):
    slot_total, blk, _ = vals.shape
    sections, _, width = feats.shape
    groups = slot_total // GROUP

    def vals_map(g, rows_ref, cols_ref, count_ref):
        last = jnp.maximum(count_ref[0] - 1, 0) // GROUP
        return (jnp.minimum(g, last), 0, 0)

    half = jax.ShapeDtypeStruct((rep_size // 2, blk, width), jnp.float32)
    half_spec = pl.BlockSpec((rep_size // 2, blk, width), lambda g, *_: (0, 0, 0))
    grid_spec = pltpu.PrefetchScalarGridSpec(
        num_scalar_prefetch=3,
        grid=(groups,),
        in_specs=[
            pl.BlockSpec((sections, blk, width), lambda g, *_: (0, 0, 0)),
            pl.BlockSpec((GROUP, blk, blk), vals_map),
        ],
        out_specs=[half_spec, half_spec],
        scratch_shapes=[pltpu.VMEM((rep_size, blk, width), jnp.float32)],
    )
    return pl.pallas_call(
        slot_kernel,
        grid_spec=grid_spec,
        out_shape=[half, half],
        compiler_params=pltpu.CompilerParams(dimension_semantics=("arbitrary",)),
        cost_estimate=pl.CostEstimate(
            flops=2 * slot_total * blk * blk * width,
            bytes_accessed=vals.size * 2 + feats.size * 2 + rep_size * blk * width * 4,
            transcendentals=0,
        ),
    )(rows, cols, count, feats, vals)


def gather_over_row(x):
    row_size = lax.axis_size("row")
    x_size = row_size // 2
    other = lax.ppermute(x, "row", [(s, (s + x_size) % row_size) for s in range(row_size)])
    pair = jnp.stack([x, other])
    parts = [pair]
    for d in range(1, x_size):
        perm = [(s, (s // x_size) * x_size + (s % x_size + d) % x_size) for s in range(row_size)]
        parts.append(lax.ppermute(pair, "row", perm))
    return jnp.concatenate(parts, axis=0)


def y_pairs(rep_size, d):
    return [(i, (i // 8) * 8 + (((i // 2) % 4 + d) % 4) * 2 + i % 2) for i in range(rep_size)]


def z_pairs(rep_size, z_size, d):
    return [(i, (((i // 8) + d) % z_size) * 8 + i % 8) for i in range(rep_size)]


def reduce_over_rep(keep, send):
    rep_size = 2 * keep.shape[0]
    z_size = rep_size // 8
    j = lax.axis_index("rep")
    y = (j // 2) % 4
    z = j // 8
    shape = (z_size, 4) + keep.shape[1:]
    keep = keep.reshape(shape)
    send = send.reshape(shape)
    early = [d for d in range(1, z_size) if d < z_size - 1]
    late = [0] + [d for d in range(1, z_size) if d not in early]
    blocks = {}
    for shifts in (early, late):
        got = lax.ppermute(
            jnp.stack(
                [lax.dynamic_index_in_dim(send, (z + d) % z_size, 0, keepdims=False) for d in shifts]
            ),
            "rep",
            [(i, i ^ 1) for i in range(rep_size)],
        )
        part = jnp.stack(
            [lax.dynamic_index_in_dim(keep, (z + d) % z_size, 0, keepdims=False) for d in shifts]
        ) + got
        acc = lax.dynamic_index_in_dim(part, y, 1, keepdims=False)
        got = [
            lax.ppermute(
                lax.dynamic_index_in_dim(part, (y + dy) % 4, 1, keepdims=False),
                "rep",
                y_pairs(rep_size, dy),
            )
            for dy in (1, 2, 3)
        ]
        for piece in got:
            acc = acc + piece
        for n, d in enumerate(shifts):
            blocks[d] = acc[n]
    out = blocks[0]
    for d in range(1, z_size):
        out = out + lax.ppermute(blocks[d], "rep", z_pairs(rep_size, z_size, d))
    return out


def layer(features, block_values, block_rows, block_cols, block_count, weight, bias):
    rep_size = lax.axis_size("rep")
    section_features = gather_over_row(features)
    device_index = lax.axis_index(("row", "rep"))
    live_count = lax.dynamic_slice_in_dim(block_count, device_index, 1, 0)
    keep, send = accumulate_slots(
        block_rows[0], block_cols[0], live_count, section_features, block_values, rep_size
    )
    summed = reduce_over_rep(keep, send)
    reduced = summed.astype(jnp.bfloat16)
    projected = jnp.dot(reduced, weight, preferred_element_type=jnp.float32) + bias
    return jax.nn.relu(projected).astype(jnp.bfloat16)


def solution(mesh):
    return jax.shard_map(
        layer,
        mesh=mesh,
        in_specs=(
            P(("row", "rep"), None),
            P(("row", "rep"), None, None),
            P(("row", "rep"), None),
            P(("row", "rep"), None),
            P(),
            P(),
            P(),
        ),
        out_specs=P(("row", "rep"), None),
        check_vma=False,
    )
```

```python
import jax
import jax.numpy as jnp
from jax import lax
from jax.experimental import pallas as pl
from jax.experimental.pallas import tpu as pltpu
from jax.sharding import PartitionSpec as P


GROUP = 64


def slot_kernel(rows_ref, cols_ref, count_ref, feats_ref, vals_ref, keep_ref, send_ref, acc_ref):
    g = pl.program_id(0)
    live = count_ref[0]
    row_index = lax.axis_index("row")
    core = lax.axis_index("rep") % 2
    x_size = feats_ref.shape[0] // 2
    lo = row_index // x_size
    xi = row_index % x_size
    row_top = acc_ref.shape[0] - 1

    @pl.when(g == 0)
    def _():
        acc_ref[...] = jnp.zeros_like(acc_ref)

    @pl.when(g * GROUP < live)
    def _():
        for s in range(GROUP):
            k = g * GROUP + s
            r = jnp.clip(rows_ref[k], 0, row_top)
            c = jnp.clip(cols_ref[k], 0, 2 * x_size - 1)
            spot = ((xi - c % x_size) % x_size) * 2 + ((c // x_size) ^ lo)
            prod = jnp.dot(vals_ref[s], feats_ref[spot], preferred_element_type=jnp.float32)
            acc_ref[r] += jnp.where(k < live, prod, 0.0)

    @pl.when(g == pl.num_programs(0) - 1)
    def _():
        for t in range(keep_ref.shape[0]):
            keep_ref[t] = acc_ref[2 * t + core]
            send_ref[t] = acc_ref[2 * t + 1 - core]


def accumulate_slots(rows, cols, count, feats, vals, rep_size):
    slot_total, blk, _ = vals.shape
    sections, _, width = feats.shape
    groups = slot_total // GROUP

    def vals_map(g, rows_ref, cols_ref, count_ref):
        last = jnp.maximum(count_ref[0] - 1, 0) // GROUP
        return (jnp.minimum(g, last), 0, 0)

    half = jax.ShapeDtypeStruct((rep_size // 2, blk, width), jnp.float32)
    half_spec = pl.BlockSpec((rep_size // 2, blk, width), lambda g, *_: (0, 0, 0))
    grid_spec = pltpu.PrefetchScalarGridSpec(
        num_scalar_prefetch=3,
        grid=(groups,),
        in_specs=[
            pl.BlockSpec((sections, blk, width), lambda g, *_: (0, 0, 0)),
            pl.BlockSpec((GROUP, blk, blk), vals_map),
        ],
        out_specs=[half_spec, half_spec],
        scratch_shapes=[pltpu.VMEM((rep_size, blk, width), jnp.float32)],
    )
    return pl.pallas_call(
        slot_kernel,
        grid_spec=grid_spec,
        out_shape=[half, half],
        compiler_params=pltpu.CompilerParams(dimension_semantics=("arbitrary",)),
        cost_estimate=pl.CostEstimate(
            flops=2 * slot_total * blk * blk * width,
            bytes_accessed=vals.size * 2 + feats.size * 2 + rep_size * blk * width * 4,
            transcendentals=0,
        ),
    )(rows, cols, count, feats, vals)


def gather_over_row(x):
    row_size = lax.axis_size("row")
    x_size = row_size // 2

    def shift(d):
        return [(s, (s // x_size) * x_size + (s % x_size + d) % x_size) for s in range(row_size)]

    own = [lax.ppermute(x, "row", shift(d)) for d in range(1, x_size)]
    other = lax.ppermute(x, "row", [(s, (s + x_size) % row_size) for s in range(row_size)])
    parts = [jnp.stack([x, other])]
    for d in range(1, x_size):
        parts.append(jnp.stack([own[d - 1], lax.ppermute(other, "row", shift(d))]))
    return jnp.concatenate(parts, axis=0)


def y_pairs(rep_size, d):
    return [(i, (i // 8) * 8 + (((i // 2) % 4 + d) % 4) * 2 + i % 2) for i in range(rep_size)]


def z_pairs(rep_size, z_size, d):
    return [(i, (((i // 8) + d) % z_size) * 8 + i % 8) for i in range(rep_size)]


def reduce_over_rep(keep, send):
    rep_size = 2 * keep.shape[0]
    z_size = rep_size // 8
    j = lax.axis_index("rep")
    y = (j // 2) % 4
    z = j // 8
    shape = (z_size, 4) + keep.shape[1:]
    keep = keep.reshape(shape)
    send = send.reshape(shape)
    early = [d for d in range(1, z_size) if d < z_size - 1]
    late = [0] + [d for d in range(1, z_size) if d not in early]
    blocks = {}
    for shifts in (early, late):
        got = lax.ppermute(
            jnp.stack(
                [lax.dynamic_index_in_dim(send, (z + d) % z_size, 0, keepdims=False) for d in shifts]
            ),
            "rep",
            [(i, i ^ 1) for i in range(rep_size)],
        )
        part = jnp.stack(
            [lax.dynamic_index_in_dim(keep, (z + d) % z_size, 0, keepdims=False) for d in shifts]
        ) + got
        acc = lax.dynamic_index_in_dim(part, y, 1, keepdims=False)
        got = [
            lax.ppermute(
                lax.dynamic_index_in_dim(part, (y + dy) % 4, 1, keepdims=False),
                "rep",
                y_pairs(rep_size, dy),
            )
            for dy in (1, 2, 3)
        ]
        for piece in got:
            acc = acc + piece
        for n, d in enumerate(shifts):
            blocks[d] = acc[n]
    out = blocks[0]
    for d in range(1, z_size):
        out = out + lax.ppermute(blocks[d], "rep", z_pairs(rep_size, z_size, d))
    return out


def layer(features, block_values, block_rows, block_cols, block_count, weight, bias):
    rep_size = lax.axis_size("rep")
    section_features = gather_over_row(features)
    device_index = lax.axis_index(("row", "rep"))
    live_count = lax.dynamic_slice_in_dim(block_count, device_index, 1, 0)
    keep, send = accumulate_slots(
        block_rows[0], block_cols[0], live_count, section_features, block_values, rep_size
    )
    summed = reduce_over_rep(keep, send)
    reduced = summed.astype(jnp.bfloat16)
    projected = jnp.dot(reduced, weight, preferred_element_type=jnp.float32) + bias
    return jax.nn.relu(projected).astype(jnp.bfloat16)


def solution(mesh):
    return jax.shard_map(
        layer,
        mesh=mesh,
        in_specs=(
            P(("row", "rep"), None),
            P(("row", "rep"), None, None),
            P(("row", "rep"), None),
            P(("row", "rep"), None),
            P(),
            P(),
            P(),
        ),
        out_specs=P(("row", "rep"), None),
        check_vma=False,
    )
```

```python
import jax
import jax.numpy as jnp
from jax import lax
from jax.experimental import pallas as pl
from jax.experimental.pallas import tpu as pltpu
from jax.sharding import PartitionSpec as P


GROUP = 64


def slot_kernel(rows_ref, cols_ref, count_ref, feats_ref, vals_ref, keep_ref, send_ref, acc_ref, sems):
    g = pl.program_id(0)
    live = count_ref[0]
    row_index = lax.axis_index("row")
    core = lax.axis_index("rep") % 2
    x_size = feats_ref.shape[0] // 2
    lo = row_index // x_size
    xi = row_index % x_size
    row_top = acc_ref.shape[0] - 1

    @pl.when(g == 0)
    def _():
        acc_ref[...] = jnp.zeros_like(acc_ref)

    @pl.when(g * GROUP < live)
    def _():
        for s in range(GROUP):
            k = g * GROUP + s
            r = jnp.clip(rows_ref[k], 0, row_top)
            c = jnp.clip(cols_ref[k], 0, 2 * x_size - 1)
            spot = ((xi - c % x_size) % x_size) * 2 + ((c // x_size) ^ lo)
            prod = jnp.dot(vals_ref[s], feats_ref[spot], preferred_element_type=jnp.float32)
            acc_ref[r] += jnp.where(k < live, prod, 0.0)

    @pl.when(g == pl.num_programs(0) - 1)
    def _():
        copies = []
        for t in range(keep_ref.shape[0]):
            for n, (dst, src) in enumerate(((keep_ref, 2 * t + core), (send_ref, 2 * t + 1 - core))):
                cp = pltpu.make_async_copy(acc_ref.at[src], dst.at[t], sems.at[2 * t + n])
                cp.start()
                copies.append(cp)
        for cp in copies:
            cp.wait()


def accumulate_slots(rows, cols, count, feats, vals, rep_size):
    slot_total, blk, _ = vals.shape
    sections, _, width = feats.shape
    groups = slot_total // GROUP

    def vals_map(g, rows_ref, cols_ref, count_ref):
        last = jnp.maximum(count_ref[0] - 1, 0) // GROUP
        return (jnp.minimum(g, last), 0, 0)

    half = jax.ShapeDtypeStruct((rep_size // 2, blk, width), jnp.float32)
    half_spec = pl.BlockSpec((rep_size // 2, blk, width), lambda g, *_: (0, 0, 0))
    grid_spec = pltpu.PrefetchScalarGridSpec(
        num_scalar_prefetch=3,
        grid=(groups,),
        in_specs=[
            pl.BlockSpec((sections, blk, width), lambda g, *_: (0, 0, 0)),
            pl.BlockSpec((GROUP, blk, blk), vals_map),
        ],
        out_specs=[pl.BlockSpec(memory_space=pl.ANY)] * 2,
        scratch_shapes=[
            pltpu.VMEM((rep_size, blk, width), jnp.float32),
            pltpu.SemaphoreType.DMA((rep_size,)),
        ],
    )
    return pl.pallas_call(
        slot_kernel,
        grid_spec=grid_spec,
        out_shape=[half, half],
        compiler_params=pltpu.CompilerParams(dimension_semantics=("arbitrary",)),
        cost_estimate=pl.CostEstimate(
            flops=2 * slot_total * blk * blk * width,
            bytes_accessed=vals.size * 2 + feats.size * 2 + rep_size * blk * width * 4,
            transcendentals=0,
        ),
    )(rows, cols, count, feats, vals)


def gather_over_row(x):
    row_size = lax.axis_size("row")
    x_size = row_size // 2

    def shift(d):
        return [(s, (s // x_size) * x_size + (s % x_size + d) % x_size) for s in range(row_size)]

    own = [lax.ppermute(x, "row", shift(d)) for d in range(1, x_size)]
    other = lax.ppermute(x, "row", [(s, (s + x_size) % row_size) for s in range(row_size)])
    parts = [jnp.stack([x, other])]
    for d in range(1, x_size):
        parts.append(jnp.stack([own[d - 1], lax.ppermute(other, "row", shift(d))]))
    return jnp.concatenate(parts, axis=0)


def y_pairs(rep_size, d):
    return [(i, (i // 8) * 8 + (((i // 2) % 4 + d) % 4) * 2 + i % 2) for i in range(rep_size)]


def z_pairs(rep_size, z_size, d):
    return [(i, (((i // 8) + d) % z_size) * 8 + i % 8) for i in range(rep_size)]


def reduce_over_rep(keep, send):
    rep_size = 2 * keep.shape[0]
    z_size = rep_size // 8
    j = lax.axis_index("rep")
    y = (j // 2) % 4
    z = j // 8
    shape = (z_size, 4) + keep.shape[1:]
    keep = keep.reshape(shape)
    send = send.reshape(shape)
    early = [d for d in range(1, z_size) if d < z_size - 1]
    late = [0] + [d for d in range(1, z_size) if d not in early]
    blocks = {}
    for shifts in (early, late):
        got = lax.ppermute(
            jnp.stack(
                [lax.dynamic_index_in_dim(send, (z + d) % z_size, 0, keepdims=False) for d in shifts]
            ),
            "rep",
            [(i, i ^ 1) for i in range(rep_size)],
        )
        part = jnp.stack([lax.dynamic_index_in_dim(keep, (z + d) % z_size, 0, keepdims=False) for d in shifts]) + got
        acc = lax.dynamic_index_in_dim(part, y, 1, keepdims=False)
        got = [
            lax.ppermute(lax.dynamic_index_in_dim(part, (y + dy) % 4, 1, keepdims=False), "rep", y_pairs(rep_size, dy))
            for dy in (1, 2, 3)
        ]
        for piece in got:
            acc = acc + piece
        for n, d in enumerate(shifts):
            blocks[d] = acc[n]
    out = blocks[0]
    for d in range(1, z_size):
        out = out + lax.ppermute(blocks[d], "rep", z_pairs(rep_size, z_size, d))
    return out


def layer(features, block_values, block_rows, block_cols, block_count, weight, bias):
    rep_size = lax.axis_size("rep")
    section_features = gather_over_row(features)
    device_index = lax.axis_index(("row", "rep"))
    live_count = lax.dynamic_slice_in_dim(block_count, device_index, 1, 0)
    keep, send = accumulate_slots(
        block_rows[0], block_cols[0], live_count, section_features, block_values, rep_size
    )
    summed = reduce_over_rep(keep, send)
    reduced = summed.astype(jnp.bfloat16)
    projected = jnp.dot(reduced, weight, preferred_element_type=jnp.float32) + bias
    return jax.nn.relu(projected).astype(jnp.bfloat16)


def solution(mesh):
    return jax.shard_map(
        layer,
        mesh=mesh,
        in_specs=(
            P(("row", "rep"), None),
            P(("row", "rep"), None, None),
            P(("row", "rep"), None),
            P(("row", "rep"), None),
            P(),
            P(),
            P(),
        ),
        out_specs=P(("row", "rep"), None),
        check_vma=False,
    )
```
